32 devices in a mesh: area: 4 (over x, core), sub: 8 (over z, y).
Axes of the slice: x: 2, y: 2, z: 4, core: 2. Of those that a mesh axis runs over, the one named last changes fastest.
Arguments:
- blocks: float32 [4, 512, 64, 256], P('area', 'sub'), as said below
- pattern: int32 [4, 512, 4], P('area', 'sub'), may hold values from 0 to 511, as said below
- line_ends: int32 [4, 2, 64], P('area'), may hold values from 0 to 32767, as said below
- sources: float32 [4, 4, 32768], P(None, 'area', 'sub'), may hold values from -6 to 6
- capacity: float32 [4, 32768], P('area', 'sub'), may hold values from 0.2 to 2
- start_volt: float32 [4, 32768], P('area', 'sub'), may hold values from -6 to 6
- start_hist: float32 [4, 2, 64], P('area'), may hold values from -6 to 6
- surge: float32 [4, 64], P('area'), may hold values from 0.2 to 1
Outputs:
- volt: float32 [4, 32768], P('area', 'sub')
- hist: float32 [4, 2, 64], P('area')
The draws below stay inside these ranges and needn't reach their ends.
Inputs may be any that keep to these rules, and one draw needn't show every extreme that they name: pattern[a, r, 0] = r. Split the 512 block rows of an area into aligned groups of 64: the other entries of a row never point into the row's own group, no two of them in one group are equal, and the entries of one group point into between 27 and 28 distinct block rows of each other group, exactly 28 for some group. `line_ends`: within an area the line-end buses are distinct and rise from the first left end to the last right end. `blocks`: the diagonal of each first stored block lies in 2 to 4.
All inputs are finite; a program needn't handle non-finite values.
Results may differ from the reference program's by a relative error of at most 0.00011.
Values sent between devices are 32-bit elements; how exact they have to be, the bound alone decides.
No kernel may reach another device: no remote copies, remote signals or barrier semaphores. Data moves between devices by JAX's collectives and lax.ppermute only.
A program may use at most 64 MiB of HBM per device.

```python
import math
import jax
import jax.numpy as jnp
from jax import lax

BR_DEV = 64
BLOCK = 64
NNZ = 4
LB = 64
STEPS = 4
SWEEPS = 8
AREAS = 4
NB = 512
BUSES = 32768


def draw_blocks(key, part):
    key_off, key_diag = jax.random.split(key)
    shape = (AREAS, NB, BLOCK, NNZ * BLOCK)
    offdiag = 0.17 * jax.random.normal(key_off, shape, jnp.float32)
    diagonal = jax.random.uniform(key_diag, (AREAS, NB, BLOCK, 1), jnp.float32, 2.0, 4.0)
    marker = jnp.arange(BLOCK)[:, None] == jnp.arange(NNZ * BLOCK)[None, :]
    return jnp.where(marker, diagonal, offdiag)


def draw_pattern(key, part):
    groups = NB // BR_DEV
    slots = BR_DEV * (NNZ - 1)
    key_slots, key_shift, key_pool = jax.random.split(key, 3)
    slot_scores = jax.random.randint(key_slots, (AREAS, groups, slots), 0, 1 << 16, dtype=jnp.int32)
    slot_scores = slot_scores * slots + jnp.arange(slots, dtype=jnp.int32)
    slot_order = jnp.argsort(slot_scores, axis=-1).astype(jnp.int32)
    shift_amount = jax.random.randint(key_shift, (AREAS, groups, 1), 0, groups - 1, dtype=jnp.int32)
    residue = (slot_order + shift_amount) % (groups - 1)
    rank_in_source = slot_order // (groups - 1)
    own_group = jnp.arange(groups, dtype=jnp.int32)[None, :, None]
    source_group = (own_group + 1 + residue) % groups
    pool_scores = jax.random.randint(key_pool, (AREAS, groups, groups, BR_DEV), 0, 1 << 16, dtype=jnp.int32)
    pool_scores = pool_scores * BR_DEV + jnp.arange(BR_DEV, dtype=jnp.int32)
    pool_order = jnp.argsort(pool_scores, axis=-1).astype(jnp.int32)
    flat_pool = pool_order.reshape(AREAS, groups, groups * BR_DEV)
    local_pick = jnp.take_along_axis(flat_pool, source_group * BR_DEV + rank_in_source, axis=2)
    column = source_group * BR_DEV + local_pick
    others = column.reshape(AREAS, NB, NNZ - 1)
    rowids = jnp.arange(NB, dtype=jnp.int32)
    first = jnp.broadcast_to(rowids[None, :, None], (AREAS, NB, 1))
    return jnp.concatenate([first, others], axis=2).astype(jnp.int32)


def draw_line_ends(key, part):
    stride = BUSES // (2 * LB)
    base = jnp.arange(2 * LB, dtype=jnp.int32) * stride
    offsets = jax.random.randint(key, (AREAS, 2 * LB), 0, stride, dtype=jnp.int32)
    chosen = base[None, :] + offsets
    chosen = chosen.at[0, 0].set(0)
    chosen = chosen.at[0, 2 * LB - 1].set(BUSES - 1)
    return chosen.reshape(AREAS, 2, LB).astype(jnp.int32)


def block_scale(own_key, shape, shards, low, largest):
    factor_of = 1.0
    for axis_at, shards_of in shards:
        draws = jax.random.uniform(jax.random.fold_in(jax.random.fold_in(own_key, 6), axis_at), (shards_of,), jnp.float32, low / len(shards), largest / len(shards))
        factor_of = factor_of * jnp.repeat(jnp.exp(draws), shape[axis_at] // shards_of).reshape((-1,) + (1,) * (len(shape) - 1 - axis_at))
    return factor_of


def noise(stream_key, shape, spread, most, shards=(), kind=jnp.bfloat16):
    factor_of = block_scale(stream_key, shape, shards, -0.22, 0.18) if shards else 1.0
    entries = jax.random.normal(stream_key, shape, jnp.float32) * spread * factor_of
    return jnp.minimum(jnp.maximum(entries, -most), most).astype(kind)


def setup_inputs(seed: int = 0) -> dict:
    splits = jax.random.split(jax.random.key(seed), 9)
    blocks = draw_blocks(jax.random.fold_in(splits[8], 71), 0)
    pattern = draw_pattern(jax.random.fold_in(splits[8], 71), 0)
    line_ends = draw_line_ends(jax.random.fold_in(splits[8], 71), 0)
    sources = noise(splits[3], (STEPS, AREAS, BUSES), 1.0, 6.0, ((1, 4), (2, 8)), jnp.float32)
    capacity = jnp.clip(jnp.exp(math.log(2.0) - 2.3025851 * jax.random.uniform(splits[4], (AREAS, BUSES), jnp.float32) ** block_scale(splits[4], (AREAS, BUSES), ((0, 4), (1, 8)), -0.2, 0.2)), 0.2, 2.0)
    start_volt = noise(splits[5], (AREAS, BUSES), 1.0, 6.0, ((0, 4), (1, 8)), jnp.float32)
    start_hist = noise(splits[6], (AREAS, 2, LB), 1.0, 6.0, ((0, 4),), jnp.float32)
    surge = jnp.clip(jnp.exp(math.log(1.0) - 1.609438 * jax.random.uniform(splits[7], (AREAS, LB), jnp.float32) ** block_scale(splits[7], (AREAS, LB), ((0, 4),), -0.2, 0.2)), 0.2, 1.0)
    return {"blocks": blocks, "pattern": pattern, "line_ends": line_ends, "sources": sources, "capacity": capacity, "start_volt": start_volt, "start_hist": start_hist, "surge": surge}


def product(blocks, pattern, field):
    areas = field.shape[0]
    width = blocks.shape[2]
    nblk = blocks.shape[1]
    field_blocks = field.reshape(areas, nblk, width)
    picked = jax.vmap(lambda xa, pa: xa[pa])(field_blocks, pattern)
    picked = picked.reshape(areas, nblk, -1)
    result = jnp.einsum("arik,ark->ari", blocks, picked, precision=lax.Precision.HIGHEST)
    return result.reshape(areas, -1)


def reference(blocks, pattern, line_ends, sources, capacity, start_volt, start_hist, surge):
    areas = start_volt.shape[0]
    width = blocks.shape[2]
    diag = jnp.diagonal(blocks[..., :width], axis1=2, axis2=3).reshape(areas, -1)
    system_diag = diag + capacity
    volt = start_volt
    hist = start_hist
    flat_ends = line_ends.reshape(areas, -1)
    for step in range(STEPS):
        rhs = sources[step] + capacity * volt
        rhs = jax.vmap(lambda r, e, h: r.at[e].add(-h))(rhs, flat_ends, hist.reshape(areas, -1))
        field = volt
        for sweep in range(SWEEPS):
            field = field + (rhs - product(blocks, pattern, field) - capacity * field) / system_diag
        volt = field
        end_volt = jax.vmap(lambda va, ea: va[ea])(volt, line_ends)
        message = -2.0 * surge * end_volt[:, 1] - hist[:, 1]
        new_left = jnp.roll(message, 1, axis=0)
        from_right_volt = jnp.roll(end_volt[:, 0], -1, axis=0)
        from_right_hist = jnp.roll(hist[:, 0], -1, axis=0)
        new_right = -2.0 * surge * from_right_volt - from_right_hist
        hist = jnp.stack([new_left, new_right], axis=1)
    return volt, hist
```

```python
import jax
import jax.numpy as jnp
from jax import lax
from jax.sharding import PartitionSpec as P

STEPS = 4
SWEEPS = 8


def shifted(value, axis, steps):
    count = lax.axis_size(axis)
    pairs = [(source, (source + steps) % count) for source in range(count)]
    return lax.ppermute(value, axis, pairs)


def collect(value):
    count = lax.axis_size("sub")
    parts = [value] + [shifted(value, "sub", k) for k in range(1, count)]
    return jnp.stack(parts)


def rotated(index, me, count, chunk):
    owner = index // chunk
    slot = (me - owner) % count
    return slot * chunk + index % chunk


def apply_blocks(blocks, own_part, others):
    picked = jnp.concatenate([own_part, others], axis=1)
    result = jnp.einsum("rik,rk->ri", blocks[0], picked, precision=lax.Precision.HIGHEST)
    return result.reshape(1, -1)


def next_hist(end_volt, hist, surge):
    message = -2.0 * surge * end_volt[:, 1] - hist[:, 1]
    new_left = shifted(message, "area", 1)
    outgoing_ends = jnp.stack([end_volt[:, 0], hist[:, 0]], axis=1)
    from_right = shifted(outgoing_ends, "area", -1)
    new_right = -2.0 * surge * from_right[:, 0] - from_right[:, 1]
    return jnp.stack([new_left, new_right], axis=1)


def on_device(blocks, pattern, line_ends, sources, capacity, start_volt, start_hist, surge):
    width = blocks.shape[2]
    rows_here = blocks.shape[1]
    local_count = rows_here * width
    count = lax.axis_size("sub")
    me = lax.axis_index("sub")
    offset = me * local_count
    diag = jnp.diagonal(blocks[..., :width], axis1=2, axis2=3).reshape(1, local_count)
    system_diag = diag + capacity
    remote_cols = rotated(pattern[0][:, 1:].reshape(-1), me, count, rows_here)
    end_index = rotated(line_ends[0], me, count, local_count)
    local_ends = line_ends - offset
    inside = (local_ends >= 0) & (local_ends < local_count)
    safe_ends = jnp.clip(local_ends, 0, local_count - 1)
    volt = start_volt
    hist = start_hist
    for step in range(STEPS):
        field = volt
        rhs = None
        for sweep in range(SWEEPS):
            whole = collect(field)
            if rhs is None:
                if step > 0:
                    end_volt = whole.reshape(-1)[end_index][None]
                    hist = next_hist(end_volt, hist, surge)
                rhs = sources[step] + capacity * volt
                inject = jnp.where(inside, -hist, 0.0)
                rhs = rhs.at[0, safe_ends.reshape(-1)].add(inject.reshape(-1))
            own_part = field.reshape(rows_here, width)
            others = whole.reshape(-1, width)[remote_cols]
            others = others.reshape(rows_here, -1)
            result = apply_blocks(blocks, own_part, others)
            field = field + (rhs - result - capacity * field) / system_diag
        volt = field
    partial_volt = jnp.where(inside, volt[0][safe_ends[0]][None], 0.0)
    end_volt = jnp.sum(collect(partial_volt), axis=0)
    hist = next_hist(end_volt, hist, surge)
    return (volt, hist)


def solution(mesh):
    in_specs = (
        P("area", "sub", None, None),
        P("area", "sub", None),
        P("area", None, None),
        P(None, "area", "sub"),
        P("area", "sub"),
        P("area", "sub"),
        P("area", None, None),
        P("area", None),
    )
    out_specs = (P("area", "sub"), P("area", None, None))
    return jax.shard_map(
        on_device, mesh=mesh, in_specs=in_specs, out_specs=out_specs, check_vma=False
    )
```

```python
import jax
import jax.numpy as jnp
from jax import lax
from jax.sharding import PartitionSpec as P

STEPS = 4
SWEEPS = 8


def shifted(value, axis, steps):
    count = lax.axis_size(axis)
    pairs = [(source, (source + steps) % count) for source in range(count)]
    return lax.ppermute(value, axis, pairs)


def collect(value):
    count = lax.axis_size("sub")
    copies = jnp.broadcast_to(value[None], (count,) + value.shape)
    return lax.all_to_all(copies, "sub", 0, 0, tiled=True)


def apply_blocks(blocks, own_part, others):
    picked = jnp.concatenate([own_part, others], axis=1)
    result = jnp.einsum("rik,rk->ri", blocks[0], picked, precision=lax.Precision.HIGHEST)
    return result.reshape(1, -1)


def next_hist(end_volt, hist, surge):
    message = -2.0 * surge * end_volt[:, 1] - hist[:, 1]
    new_left = shifted(message, "area", 1)
    outgoing_ends = jnp.stack([end_volt[:, 0], hist[:, 0]], axis=1)
    from_right = shifted(outgoing_ends, "area", -1)
    new_right = -2.0 * surge * from_right[:, 0] - from_right[:, 1]
    return jnp.stack([new_left, new_right], axis=1)


def on_device(blocks, pattern, line_ends, sources, capacity, start_volt, start_hist, surge):
    width = blocks.shape[2]
    rows_here = blocks.shape[1]
    local_count = rows_here * width
    offset = lax.axis_index("sub") * local_count
    diag = jnp.diagonal(blocks[..., :width], axis1=2, axis2=3).reshape(1, local_count)
    system_diag = diag + capacity
    remote_cols = pattern[0][:, 1:].reshape(-1)
    end_index = line_ends[0]
    local_ends = line_ends - offset
    inside = (local_ends >= 0) & (local_ends < local_count)
    safe_ends = jnp.clip(local_ends, 0, local_count - 1)
    volt = start_volt
    hist = start_hist
    for step in range(STEPS):
        field = volt
        rhs = None
        for sweep in range(SWEEPS):
            whole = collect(field)
            if rhs is None:
                if step > 0:
                    end_volt = whole.reshape(-1)[end_index][None]
                    hist = next_hist(end_volt, hist, surge)
                rhs = sources[step] + capacity * volt
                inject = jnp.where(inside, -hist, 0.0)
                rhs = rhs.at[0, safe_ends.reshape(-1)].add(inject.reshape(-1))
            own_part = field.reshape(rows_here, width)
            others = whole.reshape(-1, width)[remote_cols]
            others = others.reshape(rows_here, -1)
            result = apply_blocks(blocks, own_part, others)
            field = field + (rhs - result - capacity * field) / system_diag
        volt = field
    partial_volt = jnp.where(inside, volt[0][safe_ends[0]][None], 0.0)
    end_volt = jnp.sum(collect(partial_volt), axis=0)
    hist = next_hist(end_volt, hist, surge)
    return (volt, hist)


def solution(mesh):
    in_specs = (
        P("area", "sub", None, None),
        P("area", "sub", None),
        P("area", None, None),
        P(None, "area", "sub"),
        P("area", "sub"),
        P("area", "sub"),
        P("area", None, None),
        P("area", None),
    )
    out_specs = (P("area", "sub"), P("area", None, None))
    return jax.shard_map(
        on_device, mesh=mesh, in_specs=in_specs, out_specs=out_specs, check_vma=False
    )
```

```python
import jax
import jax.numpy as jnp
from jax import lax
from jax.sharding import PartitionSpec as P

STEPS = 4
SWEEPS = 8


def shifted(value, axis, steps):
    count = lax.axis_size(axis)
    pairs = [(source, (source + steps) % count) for source in range(count)]
    return lax.ppermute(value, axis, pairs)


def collect(value):
    count = lax.axis_size("sub")
    copies = jnp.broadcast_to(value[None], (count,) + value.shape)
    return lax.all_to_all(copies, "sub", 0, 0, tiled=True)


def apply_blocks(blocks, own_part, others):
    picked = jnp.concatenate([own_part, others], axis=1)
    result = jnp.sum(blocks[0] * picked[:, None, :], axis=2)
    return result.reshape(1, -1)


def next_hist(end_volt, hist, surge):
    message = -2.0 * surge * end_volt[:, 1] - hist[:, 1]
    new_left = shifted(message, "area", 1)
    outgoing_ends = jnp.stack([end_volt[:, 0], hist[:, 0]], axis=1)
    from_right = shifted(outgoing_ends, "area", -1)
    new_right = -2.0 * surge * from_right[:, 0] - from_right[:, 1]
    return jnp.stack([new_left, new_right], axis=1)


def on_device(blocks, pattern, line_ends, sources, capacity, start_volt, start_hist, surge):
    width = blocks.shape[2]
    rows_here = blocks.shape[1]
    local_count = rows_here * width
    offset = lax.axis_index("sub") * local_count
    diag = jnp.diagonal(blocks[..., :width], axis1=2, axis2=3).reshape(1, local_count)
    system_diag = diag + capacity
    remote_cols = pattern[0][:, 1:].reshape(-1)
    end_index = line_ends[0]
    local_ends = line_ends - offset
    inside = (local_ends >= 0) & (local_ends < local_count)
    safe_ends = jnp.clip(local_ends, 0, local_count - 1)
    volt = start_volt
    hist = start_hist
    for step in range(STEPS):
        field = volt
        rhs = None
        for sweep in range(SWEEPS):
            whole = collect(field)
            if rhs is None:
                if step > 0:
                    end_volt = whole.reshape(-1)[end_index][None]
                    hist = next_hist(end_volt, hist, surge)
                rhs = sources[step] + capacity * volt
                inject = jnp.where(inside, -hist, 0.0)
                rhs = rhs.at[0, safe_ends.reshape(-1)].add(inject.reshape(-1))
            own_part = field.reshape(rows_here, width)
            others = whole.reshape(-1, width)[remote_cols]
            others = others.reshape(rows_here, -1)
            result = apply_blocks(blocks, own_part, others)
            field = field + (rhs - result - capacity * field) / system_diag
        volt = field
    partial_volt = jnp.where(inside, volt[0][safe_ends[0]][None], 0.0)
    end_volt = jnp.sum(collect(partial_volt), axis=0)
    hist = next_hist(end_volt, hist, surge)
    return (volt, hist)


def solution(mesh):
    in_specs = (
        P("area", "sub", None, None),
        P("area", "sub", None),
        P("area", None, None),
        P(None, "area", "sub"),
        P("area", "sub"),
        P("area", "sub"),
        P("area", None, None),
        P("area", None),
    )
    out_specs = (P("area", "sub"), P("area", None, None))
    return jax.shard_map(
        on_device, mesh=mesh, in_specs=in_specs, out_specs=out_specs, check_vma=False
    )
```

```python
import jax
import jax.numpy as jnp
from jax import lax
from jax.sharding import PartitionSpec as P
from jax.experimental.layout import Layout, with_layout_constraint

STEPS = 4
SWEEPS = 8


def shifted(value, axis, steps):
    count = lax.axis_size(axis)
    pairs = [(source, (source + steps) % count) for source in range(count)]
    return lax.ppermute(value, axis, pairs)


def collect(value):
    count = lax.axis_size("sub")
    copies = jnp.broadcast_to(value[None], (count,) + value.shape)
    return lax.all_to_all(copies, "sub", 0, 0, tiled=True)


def paired_blocks(blocks):
    rows, width, depth = blocks.shape[1:]
    paired = blocks[0].reshape(rows // 2, 2, width, depth).transpose(0, 3, 1, 2)
    paired = paired.reshape(rows // 2, depth, 2 * width)
    return with_layout_constraint(paired, Layout((0, 1, 2)))


def apply_blocks(paired, own_part, others):
    picked = jnp.concatenate([own_part, others], axis=1)
    rows, depth = picked.shape
    width = paired.shape[2] // 2
    spread = picked.reshape(rows // 2, 2, depth).transpose(0, 2, 1)
    spread = jnp.broadcast_to(spread[..., None], (rows // 2, depth, 2, width))
    spread = spread.reshape(rows // 2, depth, 2 * width)
    result = jnp.sum(paired * spread, axis=1)
    return result.reshape(1, -1)


def next_hist(end_volt, hist, surge):
    message = -2.0 * surge * end_volt[:, 1] - hist[:, 1]
    new_left = shifted(message, "area", 1)
    outgoing_ends = jnp.stack([end_volt[:, 0], hist[:, 0]], axis=1)
    from_right = shifted(outgoing_ends, "area", -1)
    new_right = -2.0 * surge * from_right[:, 0] - from_right[:, 1]
    return jnp.stack([new_left, new_right], axis=1)


def on_device(blocks, pattern, line_ends, sources, capacity, start_volt, start_hist, surge):
    width = blocks.shape[2]
    rows_here = blocks.shape[1]
    local_count = rows_here * width
    offset = lax.axis_index("sub") * local_count
    diag = jnp.diagonal(blocks[..., :width], axis1=2, axis2=3).reshape(1, local_count)
    system_diag = diag + capacity
    paired = paired_blocks(blocks)
    remote_cols = pattern[0][:, 1:].reshape(-1)
    end_index = line_ends[0]
    local_ends = line_ends - offset
    inside = (local_ends >= 0) & (local_ends < local_count)
    safe_ends = jnp.clip(local_ends, 0, local_count - 1)
    volt = start_volt
    hist = start_hist
    for step in range(STEPS):
        field = volt
        rhs = None
        for sweep in range(SWEEPS):
            whole = collect(field)
            if rhs is None:
                if step > 0:
                    end_volt = whole.reshape(-1)[end_index][None]
                    hist = next_hist(end_volt, hist, surge)
                rhs = sources[step] + capacity * volt
                inject = jnp.where(inside, -hist, 0.0)
                rhs = rhs.at[0, safe_ends.reshape(-1)].add(inject.reshape(-1))
            own_part = field.reshape(rows_here, width)
            others = whole.reshape(-1, width)[remote_cols]
            others = others.reshape(rows_here, -1)
            result = apply_blocks(paired, own_part, others)
            field = field + (rhs - result - capacity * field) / system_diag
        volt = field
    partial_volt = jnp.where(inside, volt[0][safe_ends[0]][None], 0.0)
    end_volt = jnp.sum(collect(partial_volt), axis=0)
    hist = next_hist(end_volt, hist, surge)
    return (volt, hist)


def solution(mesh):
    in_specs = (
        P("area", "sub", None, None),
        P("area", "sub", None),
        P("area", None, None),
        P(None, "area", "sub"),
        P("area", "sub"),
        P("area", "sub"),
        P("area", None, None),
        P("area", None),
    )
    out_specs = (P("area", "sub"), P("area", None, None))
    return jax.shard_map(
        on_device, mesh=mesh, in_specs=in_specs, out_specs=out_specs, check_vma=False
    )
```

```python
import jax
import jax.numpy as jnp
from jax import lax
from jax.sharding import PartitionSpec as P

STEPS = 4
SWEEPS = 8


def shifted(value, axis, steps):
    count = lax.axis_size(axis)
    pairs = [(source, (source + steps) % count) for source in range(count)]
    return lax.ppermute(value, axis, pairs)


def collect(value):
    count = lax.axis_size("sub")
    copies = jnp.broadcast_to(value[None], (count,) + value.shape)
    return lax.all_to_all(copies, "sub", 0, 0, tiled=True)


def next_hist(end_volt, hist, surge):
    message = -2.0 * surge * end_volt[:, 1] - hist[:, 1]
    new_left = shifted(message, "area", 1)
    outgoing_ends = jnp.stack([end_volt[:, 0], hist[:, 0]], axis=1)
    from_right = shifted(outgoing_ends, "area", -1)
    new_right = -2.0 * surge * from_right[:, 0] - from_right[:, 1]
    return jnp.stack([new_left, new_right], axis=1)


def on_device(blocks, pattern, line_ends, sources, capacity, start_volt, start_hist, surge):
    width = blocks.shape[2]
    rows_here = blocks.shape[1]
    local_count = rows_here * width
    shape = (1, local_count)
    offset = lax.axis_index("sub") * local_count
    diag = jnp.diagonal(blocks[0, :, :, :width], axis1=1, axis2=2).reshape(shape)
    capacity = capacity.reshape(shape)
    system_diag = diag + capacity
    own_blocks = blocks[0, :, :, :width]
    remote_blocks = blocks[0, :, :, width:]
    remote_cols = pattern[0][:, 1:].reshape(-1)
    end_index = line_ends[0]
    local_ends = line_ends - offset
    inside = (local_ends >= 0) & (local_ends < local_count)
    safe_ends = jnp.clip(local_ends, 0, local_count - 1)
    field = start_volt.reshape(shape)
    hist = start_hist
    for step in range(STEPS):
        rhs = None
        for sweep in range(SWEEPS):
            whole = collect(field)
            own_part = field.reshape(rows_here, width)
            own = jnp.sum(own_blocks * own_part[:, None, :], axis=2).reshape(shape)
            pre = capacity * field + own
            if rhs is None:
                if step > 0:
                    end_volt = whole.reshape(-1)[end_index][None]
                    hist = next_hist(end_volt, hist, surge)
                rhs = sources[step].reshape(shape) + capacity * field
                inject = jnp.where(inside, -hist, 0.0)
                rhs = rhs.reshape(-1).at[safe_ends.reshape(-1)].add(inject.reshape(-1))
                rhs = rhs.reshape(shape)
            others = whole.reshape(-1, width)[remote_cols].reshape(rows_here, -1)
            remote = jnp.sum(remote_blocks * others[:, None, :], axis=2).reshape(shape)
            field = field + (rhs - pre - remote) / system_diag
    partial_volt = jnp.where(inside, field.reshape(-1)[safe_ends[0]][None], 0.0)
    end_volt = jnp.sum(collect(partial_volt), axis=0)
    hist = next_hist(end_volt, hist, surge)
    return (field, hist)


def solution(mesh):
    in_specs = (
        P("area", "sub", None, None),
        P("area", "sub", None),
        P("area", None, None),
        P(None, "area", "sub"),
        P("area", "sub"),
        P("area", "sub"),
        P("area", None, None),
        P("area", None),
    )
    out_specs = (P("area", "sub"), P("area", None, None))
    return jax.shard_map(
        on_device, mesh=mesh, in_specs=in_specs, out_specs=out_specs, check_vma=False
    )
```

```python
import jax
import jax.numpy as jnp
from jax import lax
from jax.sharding import PartitionSpec as P

STEPS = 4
SWEEPS = 8


def shifted(value, axis, steps):
    count = lax.axis_size(axis)
    pairs = [(source, (source + steps) % count) for source in range(count)]
    return lax.ppermute(value, axis, pairs)


def collect(value):
    count = lax.axis_size("sub")
    half = count // 2
    partner = lax.ppermute(value, "sub", [(i, i ^ 1) for i in range(count)])
    pair = jnp.stack([value, partner])
    parts = [pair]
    for k in range(1, half):
        moves = [(i, ((i // 2 + k) % half) * 2 + i % 2) for i in range(count)]
        parts.append(lax.ppermute(pair, "sub", moves))
    return jnp.stack(parts).reshape((count,) + value.shape)


def slot_of(index, me, count, chunk):
    owner = index // chunk
    slot = ((me // 2 - owner // 2) % (count // 2)) * 2 + ((owner % 2) ^ (me % 2))
    return slot * chunk + index % chunk


def apply_blocks(blocks, own_part, others):
    picked = jnp.concatenate([own_part, others], axis=1)
    result = jnp.sum(blocks[0] * picked[:, None, :], axis=2)
    return result.reshape(1, -1)


def next_hist(end_volt, hist, surge):
    message = -2.0 * surge * end_volt[:, 1] - hist[:, 1]
    new_left = shifted(message, "area", 1)
    outgoing_ends = jnp.stack([end_volt[:, 0], hist[:, 0]], axis=1)
    from_right = shifted(outgoing_ends, "area", -1)
    new_right = -2.0 * surge * from_right[:, 0] - from_right[:, 1]
    return jnp.stack([new_left, new_right], axis=1)


def on_device(blocks, pattern, line_ends, sources, capacity, start_volt, start_hist, surge):
    width = blocks.shape[2]
    rows_here = blocks.shape[1]
    local_count = rows_here * width
    offset = lax.axis_index("sub") * local_count
    diag = jnp.diagonal(blocks[..., :width], axis1=2, axis2=3).reshape(1, local_count)
    system_diag = diag + capacity
    count = lax.axis_size("sub")
    me = lax.axis_index("sub")
    remote_cols = slot_of(pattern[0][:, 1:].reshape(-1), me, count, rows_here)
    end_index = slot_of(line_ends[0], me, count, local_count)
    local_ends = line_ends - offset
    inside = (local_ends >= 0) & (local_ends < local_count)
    safe_ends = jnp.clip(local_ends, 0, local_count - 1)
    volt = start_volt
    hist = start_hist
    for step in range(STEPS):
        field = volt
        rhs = None
        for sweep in range(SWEEPS):
            whole = collect(field)
            if rhs is None:
                if step > 0:
                    end_volt = whole.reshape(-1)[end_index][None]
                    hist = next_hist(end_volt, hist, surge)
                rhs = sources[step] + capacity * volt
                inject = jnp.where(inside, -hist, 0.0)
                rhs = rhs.at[0, safe_ends.reshape(-1)].add(inject.reshape(-1))
            own_part = field.reshape(rows_here, width)
            others = whole.reshape(-1, width)[remote_cols]
            others = others.reshape(rows_here, -1)
            result = apply_blocks(blocks, own_part, others)
            field = field + (rhs - result - capacity * field) / system_diag
        volt = field
    partial_volt = jnp.where(inside, volt[0][safe_ends[0]][None], 0.0)
    end_volt = jnp.sum(collect(partial_volt), axis=0)
    hist = next_hist(end_volt, hist, surge)
    return (volt, hist)


def solution(mesh):
    in_specs = (
        P("area", "sub", None, None),
        P("area", "sub", None),
        P("area", None, None),
        P(None, "area", "sub"),
        P("area", "sub"),
        P("area", "sub"),
        P("area", None, None),
        P("area", None),
    )
    out_specs = (P("area", "sub"), P("area", None, None))
    return jax.shard_map(
        on_device, mesh=mesh, in_specs=in_specs, out_specs=out_specs, check_vma=False
    )
```

```python
import jax
import jax.numpy as jnp
from jax import lax
from jax.sharding import PartitionSpec as P

STEPS = 4
SWEEPS = 8


def shifted(value, axis, steps):
    count = lax.axis_size(axis)
    pairs = [(source, (source + steps) % count) for source in range(count)]
    return lax.ppermute(value, axis, pairs)


def collect(value):
    count = lax.axis_size("sub")
    half = count // 2
    parts = [value]
    for k in range(1, half):
        moves = [(i, ((i // 2 + k) % half) * 2 + i % 2) for i in range(count)]
        parts.append(lax.ppermute(value, "sub", moves))
    group = jnp.stack(parts)
    partner = lax.ppermute(group, "sub", [(i, i ^ 1) for i in range(count)])
    return jnp.stack([group, partner]).reshape((count,) + value.shape)


def slot_of(index, me, count, chunk):
    owner = index // chunk
    half = count // 2
    slot = ((owner % 2) ^ (me % 2)) * half + (me // 2 - owner // 2) % half
    return slot * chunk + index % chunk


def apply_blocks(blocks, own_part, others):
    picked = jnp.concatenate([own_part, others], axis=1)
    result = jnp.sum(blocks[0] * picked[:, None, :], axis=2)
    return result.reshape(1, -1)


def next_hist(end_volt, hist, surge):
    message = -2.0 * surge * end_volt[:, 1] - hist[:, 1]
    new_left = shifted(message, "area", 1)
    outgoing_ends = jnp.stack([end_volt[:, 0], hist[:, 0]], axis=1)
    from_right = shifted(outgoing_ends, "area", -1)
    new_right = -2.0 * surge * from_right[:, 0] - from_right[:, 1]
    return jnp.stack([new_left, new_right], axis=1)


def on_device(blocks, pattern, line_ends, sources, capacity, start_volt, start_hist, surge):
    width = blocks.shape[2]
    rows_here = blocks.shape[1]
    local_count = rows_here * width
    offset = lax.axis_index("sub") * local_count
    diag = jnp.diagonal(blocks[..., :width], axis1=2, axis2=3).reshape(1, local_count)
    system_diag = diag + capacity
    count = lax.axis_size("sub")
    me = lax.axis_index("sub")
    remote_cols = slot_of(pattern[0][:, 1:].reshape(-1), me, count, rows_here)
    end_index = slot_of(line_ends[0], me, count, local_count)
    local_ends = line_ends - offset
    inside = (local_ends >= 0) & (local_ends < local_count)
    safe_ends = jnp.clip(local_ends, 0, local_count - 1)
    volt = start_volt
    hist = start_hist
    for step in range(STEPS):
        field = volt
        rhs = None
        for sweep in range(SWEEPS):
            whole = collect(field)
            if rhs is None:
                if step > 0:
                    end_volt = whole.reshape(-1)[end_index][None]
                    hist = next_hist(end_volt, hist, surge)
                rhs = sources[step] + capacity * volt
                inject = jnp.where(inside, -hist, 0.0)
                rhs = rhs.at[0, safe_ends.reshape(-1)].add(inject.reshape(-1))
            own_part = field.reshape(rows_here, width)
            others = whole.reshape(-1, width)[remote_cols]
            others = others.reshape(rows_here, -1)
            result = apply_blocks(blocks, own_part, others)
            field = field + (rhs - result - capacity * field) / system_diag
        volt = field
    partial_volt = jnp.where(inside, volt[0][safe_ends[0]][None], 0.0)
    end_volt = jnp.sum(collect(partial_volt), axis=0)
    hist = next_hist(end_volt, hist, surge)
    return (volt, hist)


def solution(mesh):
    in_specs = (
        P("area", "sub", None, None),
        P("area", "sub", None),
        P("area", None, None),
        P(None, "area", "sub"),
        P("area", "sub"),
        P("area", "sub"),
        P("area", None, None),
        P("area", None),
    )
    out_specs = (P("area", "sub"), P("area", None, None))
    return jax.shard_map(
        on_device, mesh=mesh, in_specs=in_specs, out_specs=out_specs, check_vma=False
    )
```

```python
import jax
import jax.numpy as jnp
from jax import lax
from jax.sharding import PartitionSpec as P

STEPS = 4
SWEEPS = 8


def shifted(value, axis, steps):
    count = lax.axis_size(axis)
    pairs = [(source, (source + steps) % count) for source in range(count)]
    return lax.ppermute(value, axis, pairs)


def collect(value):
    count = lax.axis_size("sub")
    half = count // 2
    partner = lax.ppermute(value, "sub", [(i, i ^ 1) for i in range(count)])
    pair = jnp.stack([value, partner])
    parts = [pair]
    for k in range(1, half):
        moves = [(i, ((i // 2 + k) % half) * 2 + i % 2) for i in range(count)]
        parts.append(lax.ppermute(pair, "sub", moves))
    return jnp.stack(parts).reshape((count,) + value.shape)


def slot_of(index, me, count, chunk):
    owner = index // chunk
    slot = ((me // 2 - owner // 2) % (count // 2)) * 2 + ((owner % 2) ^ (me % 2))
    return slot * chunk + index % chunk


def apply_blocks(blocks, own_part, others):
    picked = jnp.concatenate([own_part, others], axis=1)
    result = jnp.sum(blocks[0] * picked[:, None, :], axis=2)
    return result.reshape(1, -1)


def next_hist(end_volt, hist, surge):
    message = -2.0 * surge * end_volt[:, 1] - hist[:, 1]
    new_left = shifted(message, "area", 1)
    outgoing_ends = jnp.stack([end_volt[:, 0], hist[:, 0]], axis=1)
    from_right = shifted(outgoing_ends, "area", -1)
    new_right = -2.0 * surge * from_right[:, 0] - from_right[:, 1]
    return jnp.stack([new_left, new_right], axis=1)


def on_device(blocks, pattern, line_ends, sources, capacity, start_volt, start_hist, surge):
    width = blocks.shape[2]
    rows_here = blocks.shape[1]
    local_count = rows_here * width
    offset = lax.axis_index("sub") * local_count
    eye = jnp.arange(width)[:, None] == jnp.arange(width)[None, :]
    diag = jnp.sum(jnp.where(eye, blocks[0, :, :, :width], 0.0), axis=2).reshape(1, local_count)
    system_diag = diag + capacity
    count = lax.axis_size("sub")
    me = lax.axis_index("sub")
    remote_cols = slot_of(pattern[0][:, 1:].reshape(-1), me, count, rows_here)
    end_index = slot_of(line_ends[0], me, count, local_count)
    local_ends = line_ends - offset
    inside = (local_ends >= 0) & (local_ends < local_count)
    safe_ends = jnp.clip(local_ends, 0, local_count - 1)
    volt = start_volt
    hist = start_hist
    for step in range(STEPS):
        field = volt
        rhs = None
        for sweep in range(SWEEPS):
            whole = collect(field)
            if rhs is None:
                if step > 0:
                    end_volt = whole.reshape(-1)[end_index][None]
                    hist = next_hist(end_volt, hist, surge)
                rhs = sources[step] + capacity * volt
                inject = jnp.where(inside, -hist, 0.0)
                rhs = rhs.at[0, safe_ends.reshape(-1)].add(inject.reshape(-1))
            own_part = field.reshape(rows_here, width)
            others = whole.reshape(-1, width)[remote_cols]
            others = others.reshape(rows_here, -1)
            result = apply_blocks(blocks, own_part, others)
            field = field + (rhs - result - capacity * field) / system_diag
        volt = field
    partial_volt = jnp.where(inside, volt[0][safe_ends[0]][None], 0.0)
    end_volt = jnp.sum(collect(partial_volt), axis=0)
    hist = next_hist(end_volt, hist, surge)
    return (volt, hist)


def solution(mesh):
    in_specs = (
        P("area", "sub", None, None),
        P("area", "sub", None),
        P("area", None, None),
        P(None, "area", "sub"),
        P("area", "sub"),
        P("area", "sub"),
        P("area", None, None),
        P("area", None),
    )
    out_specs = (P("area", "sub"), P("area", None, None))
    return jax.shard_map(
        on_device, mesh=mesh, in_specs=in_specs, out_specs=out_specs, check_vma=False
    )
```

```python
import jax
import jax.numpy as jnp
from jax import lax
from jax.sharding import PartitionSpec as P

STEPS = 4
SWEEPS = 8


def shifted(value, axis, steps):
    count = lax.axis_size(axis)
    pairs = [(source, (source + steps) % count) for source in range(count)]
    return lax.ppermute(value, axis, pairs)


def collect(value):
    count = lax.axis_size("sub")
    half = count // 2
    partner = lax.ppermute(value, "sub", [(i, i ^ 1) for i in range(count)])
    pair = jnp.stack([value, partner])
    parts = [pair]
    for k in range(1, half):
        moves = [(i, ((i // 2 + k) % half) * 2 + i % 2) for i in range(count)]
        parts.append(lax.ppermute(pair, "sub", moves))
    return jnp.stack(parts).reshape((count,) + value.shape)


def slot_of(index, me, count, chunk):
    owner = index // chunk
    slot = ((me // 2 - owner // 2) % (count // 2)) * 2 + ((owner % 2) ^ (me % 2))
    return slot * chunk + index % chunk


def apply_blocks(blocks, own_part, others):
    picked = jnp.concatenate([own_part, others], axis=1)
    result = jnp.sum(blocks[0] * picked[:, None, :], axis=2)
    return result.reshape(1, -1)


def next_hist(end_volt, hist, surge):
    message = -2.0 * surge * end_volt[:, 1] - hist[:, 1]
    new_left = shifted(message, "area", 1)
    outgoing_ends = jnp.stack([end_volt[:, 0], hist[:, 0]], axis=1)
    from_right = shifted(outgoing_ends, "area", -1)
    new_right = -2.0 * surge * from_right[:, 0] - from_right[:, 1]
    return jnp.stack([new_left, new_right], axis=1)


def on_device(blocks, pattern, line_ends, sources, capacity, start_volt, start_hist, surge):
    width = blocks.shape[2]
    rows_here = blocks.shape[1]
    local_count = rows_here * width
    offset = lax.axis_index("sub") * local_count
    eye = jnp.arange(width)[:, None] == jnp.arange(width)[None, :]
    diag = jnp.sum(jnp.where(eye, blocks[0, :, :, :width], 0.0), axis=2).reshape(1, local_count)
    system_diag = diag + capacity
    count = lax.axis_size("sub")
    me = lax.axis_index("sub")
    remote_cols = slot_of(pattern[0][:, 1:].reshape(-1), me, count, rows_here)
    end_index = slot_of(line_ends[0], me, count, local_count)
    local_ends = line_ends - offset
    inside = (local_ends >= 0) & (local_ends < local_count)
    safe_ends = jnp.clip(local_ends, 0, local_count - 1)
    volt = start_volt
    hist = start_hist
    for step in range(STEPS):
        field = volt
        rhs = None
        for sweep in range(SWEEPS):
            whole = collect(field.reshape(-1, 128))
            if rhs is None:
                if step > 0:
                    end_volt = whole.reshape(-1)[end_index][None]
                    hist = next_hist(end_volt, hist, surge)
                rhs = sources[step] + capacity * volt
                inject = jnp.where(inside, -hist, 0.0)
                rhs = rhs.at[0, safe_ends.reshape(-1)].add(inject.reshape(-1))
            own_part = field.reshape(rows_here, width)
            others = whole.reshape(-1, width)[remote_cols]
            others = others.reshape(rows_here, -1)
            result = apply_blocks(blocks, own_part, others)
            field = field + (rhs - result - capacity * field) / system_diag
        volt = field
    partial_volt = jnp.where(inside, volt[0][safe_ends[0]][None], 0.0)
    end_volt = jnp.sum(collect(partial_volt), axis=0)
    hist = next_hist(end_volt, hist, surge)
    return (volt, hist)


def solution(mesh):
    in_specs = (
        P("area", "sub", None, None),
        P("area", "sub", None),
        P("area", None, None),
        P(None, "area", "sub"),
        P("area", "sub"),
        P("area", "sub"),
        P("area", None, None),
        P("area", None),
    )
    out_specs = (P("area", "sub"), P("area", None, None))
    return jax.shard_map(
        on_device, mesh=mesh, in_specs=in_specs, out_specs=out_specs, check_vma=False
    )
```

```python
import jax
import jax.numpy as jnp
from jax import lax
from jax.sharding import PartitionSpec as P

STEPS = 4
SWEEPS = 8


def shifted(value, axis, steps):
    count = lax.axis_size(axis)
    pairs = [(source, (source + steps) % count) for source in range(count)]
    return lax.ppermute(value, axis, pairs)


def collect(value):
    count = lax.axis_size("sub")
    half = count // 2
    partner = lax.ppermute(value, "sub", [(i, i ^ 1) for i in range(count)])
    pair = jnp.stack([value, partner])
    parts = [pair]
    for k in range(1, half):
        moves = [(i, ((i // 2 + k) % half) * 2 + i % 2) for i in range(count)]
        parts.append(lax.ppermute(pair, "sub", moves))
    return jnp.stack(parts).reshape((count,) + value.shape)


def slot_of(index, me, count, chunk):
    owner = index // chunk
    slot = ((me // 2 - owner // 2) % (count // 2)) * 2 + ((owner % 2) ^ (me % 2))
    return slot * chunk + index % chunk


def apply_blocks(blocks, own_part, others):
    picked = jnp.concatenate([own_part, others], axis=1)
    result = jnp.sum(blocks[0] * picked[:, None, :], axis=2)
    return result.reshape(1, -1)


def next_hist(end_volt, hist, surge):
    message = -2.0 * surge * end_volt[:, 1] - hist[:, 1]
    new_left = shifted(message, "area", 1)
    outgoing_ends = jnp.stack([end_volt[:, 0], hist[:, 0]], axis=1)
    from_right = shifted(outgoing_ends, "area", -1)
    new_right = -2.0 * surge * from_right[:, 0] - from_right[:, 1]
    return jnp.stack([new_left, new_right], axis=1)


def on_device(blocks, pattern, line_ends, sources, capacity, start_volt, start_hist, surge):
    width = blocks.shape[2]
    rows_here = blocks.shape[1]
    local_count = rows_here * width
    offset = lax.axis_index("sub") * local_count
    eye = jnp.arange(width)[:, None] == jnp.arange(width)[None, :]
    diag = jnp.sum(jnp.where(eye, blocks[0, :, :, :width], 0.0), axis=2).reshape(1, local_count)
    system_diag = diag + capacity
    count = lax.axis_size("sub")
    me = lax.axis_index("sub")
    remote_cols = slot_of(pattern[0][:, 1:].reshape(-1), me, count, rows_here)
    end_index = slot_of(line_ends[0], me, count, local_count)
    local_ends = line_ends - offset
    inside = (local_ends >= 0) & (local_ends < local_count)
    safe_ends = jnp.clip(local_ends, 0, local_count - 1)
    buses = jnp.arange(local_count)[None, :]
    at_bus = (safe_ends.reshape(-1, 1) == buses) & inside.reshape(-1, 1)
    volt = start_volt
    hist = start_hist
    for step in range(STEPS):
        field = volt
        rhs = None
        for sweep in range(SWEEPS):
            whole = collect(field.reshape(-1, 128))
            if rhs is None:
                if step > 0:
                    end_volt = whole.reshape(-1)[end_index][None]
                    hist = next_hist(end_volt, hist, surge)
                rhs = sources[step] + capacity * volt
                inject = jnp.where(at_bus, -hist.reshape(-1, 1), 0.0)
                rhs = rhs + jnp.sum(inject, axis=0, keepdims=True)
            own_part = field.reshape(rows_here, width)
            others = whole.reshape(-1, width)[remote_cols]
            others = others.reshape(rows_here, -1)
            result = apply_blocks(blocks, own_part, others)
            field = field + (rhs - result - capacity * field) / system_diag
        volt = field
    partial_volt = jnp.where(inside, volt[0][safe_ends[0]][None], 0.0)
    end_volt = jnp.sum(collect(partial_volt), axis=0)
    hist = next_hist(end_volt, hist, surge)
    return (volt, hist)


def solution(mesh):
    in_specs = (
        P("area", "sub", None, None),
        P("area", "sub", None),
        P("area", None, None),
        P(None, "area", "sub"),
        P("area", "sub"),
        P("area", "sub"),
        P("area", None, None),
        P("area", None),
    )
    out_specs = (P("area", "sub"), P("area", None, None))
    return jax.shard_map(
        on_device, mesh=mesh, in_specs=in_specs, out_specs=out_specs, check_vma=False
    )
```

```python
import jax
import jax.numpy as jnp
from jax import lax
from jax.sharding import PartitionSpec as P

STEPS = 4
SWEEPS = 8


def shifted(value, axis, steps):
    count = lax.axis_size(axis)
    pairs = [(source, (source + steps) % count) for source in range(count)]
    return lax.ppermute(value, axis, pairs)


def collect(value):
    count = lax.axis_size("sub")
    half = count // 2
    partner = lax.ppermute(value, "sub", [(i, i ^ 1) for i in range(count)])
    pair = jnp.stack([value, partner])
    parts = [pair]
    for k in range(1, half):
        moves = [(i, ((i // 2) ^ k) * 2 + i % 2) for i in range(count)]
        parts.append(lax.ppermute(pair, "sub", moves))
    return jnp.stack(parts).reshape((count,) + value.shape)


def slot_of(index, me, count, chunk):
    owner = index // chunk
    slot = ((me // 2) ^ (owner // 2)) * 2 + ((owner % 2) ^ (me % 2))
    return slot * chunk + index % chunk


def apply_blocks(blocks, own_part, others):
    picked = jnp.concatenate([own_part, others], axis=1)
    result = jnp.sum(blocks[0] * picked[:, None, :], axis=2)
    return result.reshape(1, -1)


def next_hist(end_volt, hist, surge):
    message = -2.0 * surge * end_volt[:, 1] - hist[:, 1]
    new_left = shifted(message, "area", 1)
    outgoing_ends = jnp.stack([end_volt[:, 0], hist[:, 0]], axis=1)
    from_right = shifted(outgoing_ends, "area", -1)
    new_right = -2.0 * surge * from_right[:, 0] - from_right[:, 1]
    return jnp.stack([new_left, new_right], axis=1)


def on_device(blocks, pattern, line_ends, sources, capacity, start_volt, start_hist, surge):
    width = blocks.shape[2]
    rows_here = blocks.shape[1]
    local_count = rows_here * width
    offset = lax.axis_index("sub") * local_count
    eye = jnp.arange(width)[:, None] == jnp.arange(width)[None, :]
    diag = jnp.sum(jnp.where(eye, blocks[0, :, :, :width], 0.0), axis=2).reshape(1, local_count)
    system_diag = diag + capacity
    count = lax.axis_size("sub")
    me = lax.axis_index("sub")
    remote_cols = slot_of(pattern[0][:, 1:].reshape(-1), me, count, rows_here)
    end_index = slot_of(line_ends[0], me, count, local_count)
    local_ends = line_ends - offset
    inside = (local_ends >= 0) & (local_ends < local_count)
    safe_ends = jnp.clip(local_ends, 0, local_count - 1)
    buses = jnp.arange(local_count)[None, :]
    at_bus = (safe_ends.reshape(-1, 1) == buses) & inside.reshape(-1, 1)
    volt = start_volt
    hist = start_hist
    for step in range(STEPS):
        field = volt
        rhs = None
        for sweep in range(SWEEPS):
            whole = collect(field.reshape(-1, 128))
            if rhs is None:
                if step > 0:
                    end_volt = whole.reshape(-1)[end_index][None]
                    hist = next_hist(end_volt, hist, surge)
                rhs = sources[step] + capacity * volt
                inject = jnp.where(at_bus, -hist.reshape(-1, 1), 0.0)
                rhs = rhs + jnp.sum(inject, axis=0, keepdims=True)
            own_part = field.reshape(rows_here, width)
            others = whole.reshape(-1, width)[remote_cols]
            others = others.reshape(rows_here, -1)
            result = apply_blocks(blocks, own_part, others)
            field = field + (rhs - result - capacity * field) / system_diag
        volt = field
    partial_volt = jnp.where(inside, volt[0][safe_ends[0]][None], 0.0)
    end_volt = jnp.sum(collect(partial_volt), axis=0)
    hist = next_hist(end_volt, hist, surge)
    return (volt, hist)


def solution(mesh):
    in_specs = (
        P("area", "sub", None, None),
        P("area", "sub", None),
        P("area", None, None),
        P(None, "area", "sub"),
        P("area", "sub"),
        P("area", "sub"),
        P("area", None, None),
        P("area", None),
    )
    out_specs = (P("area", "sub"), P("area", None, None))
    return jax.shard_map(
        on_device, mesh=mesh, in_specs=in_specs, out_specs=out_specs, check_vma=False
    )
```

```python
import jax
import jax.numpy as jnp
from jax import lax
from jax.sharding import PartitionSpec as P

STEPS = 4
SWEEPS = 8


def shifted(value, axis, steps):
    count = lax.axis_size(axis)
    pairs = [(source, (source + steps) % count) for source in range(count)]
    return lax.ppermute(value, axis, pairs)


def collect(value):
    count = lax.axis_size("sub")
    half = count // 2
    partner = lax.ppermute(value, "sub", [(i, i ^ 1) for i in range(count)])
    pair = jnp.stack([value, partner])
    parts = [pair]
    for k in range(1, half):
        moves = [(i, ((i // 2 + k) % half) * 2 + i % 2) for i in range(count)]
        parts.append(lax.ppermute(pair, "sub", moves))
    return jnp.stack(parts).reshape((count,) + value.shape)


def slot_of(index, me, count, chunk):
    owner = index // chunk
    slot = ((me // 2 - owner // 2) % (count // 2)) * 2 + ((owner % 2) ^ (me % 2))
    return slot * chunk + index % chunk


def apply_blocks(blocks, own_part, others):
    picked = jnp.concatenate([own_part, others], axis=1)
    terms = blocks[0] * picked[:, None, :]
    lanes = 128
    folded = terms[..., :lanes]
    for start in range(lanes, terms.shape[2], lanes):
        folded = folded + terms[..., start:start + lanes]
    result = jnp.sum(folded, axis=2)
    return result.reshape(1, -1)


def next_hist(end_volt, hist, surge):
    message = -2.0 * surge * end_volt[:, 1] - hist[:, 1]
    new_left = shifted(message, "area", 1)
    outgoing_ends = jnp.stack([end_volt[:, 0], hist[:, 0]], axis=1)
    from_right = shifted(outgoing_ends, "area", -1)
    new_right = -2.0 * surge * from_right[:, 0] - from_right[:, 1]
    return jnp.stack([new_left, new_right], axis=1)


def on_device(blocks, pattern, line_ends, sources, capacity, start_volt, start_hist, surge):
    width = blocks.shape[2]
    rows_here = blocks.shape[1]
    local_count = rows_here * width
    offset = lax.axis_index("sub") * local_count
    eye = jnp.arange(width)[:, None] == jnp.arange(width)[None, :]
    diag = jnp.sum(jnp.where(eye, blocks[0, :, :, :width], 0.0), axis=2).reshape(1, local_count)
    system_diag = diag + capacity
    count = lax.axis_size("sub")
    me = lax.axis_index("sub")
    remote_cols = slot_of(pattern[0][:, 1:].reshape(-1), me, count, rows_here)
    end_index = slot_of(line_ends[0], me, count, local_count)
    local_ends = line_ends - offset
    inside = (local_ends >= 0) & (local_ends < local_count)
    safe_ends = jnp.clip(local_ends, 0, local_count - 1)
    buses = jnp.arange(local_count)[None, :]
    at_bus = (safe_ends.reshape(-1, 1) == buses) & inside.reshape(-1, 1)
    volt = start_volt
    hist = start_hist
    for step in range(STEPS):
        field = volt
        rhs = None
        for sweep in range(SWEEPS):
            whole = collect(field.reshape(-1, 128))
            if rhs is None:
                if step > 0:
                    end_volt = whole.reshape(-1)[end_index][None]
                    hist = next_hist(end_volt, hist, surge)
                rhs = sources[step] + capacity * volt
                inject = jnp.where(at_bus, -hist.reshape(-1, 1), 0.0)
                rhs = rhs + jnp.sum(inject, axis=0, keepdims=True)
            own_part = field.reshape(rows_here, width)
            others = whole.reshape(-1, width)[remote_cols]
            others = others.reshape(rows_here, -1)
            result = apply_blocks(blocks, own_part, others)
            field = field + (rhs - result - capacity * field) / system_diag
        volt = field
    partial_volt = jnp.where(inside, volt[0][safe_ends[0]][None], 0.0)
    end_volt = jnp.sum(collect(partial_volt), axis=0)
    hist = next_hist(end_volt, hist, surge)
    return (volt, hist)


def solution(mesh):
    in_specs = (
        P("area", "sub", None, None),
        P("area", "sub", None),
        P("area", None, None),
        P(None, "area", "sub"),
        P("area", "sub"),
        P("area", "sub"),
        P("area", None, None),
        P("area", None),
    )
    out_specs = (P("area", "sub"), P("area", None, None))
    return jax.shard_map(
        on_device, mesh=mesh, in_specs=in_specs, out_specs=out_specs, check_vma=False
    )
```

```python
import jax
import jax.numpy as jnp
from jax import lax
from jax.sharding import PartitionSpec as P

STEPS = 4
SWEEPS = 8


def shifted(value, axis, steps):
    count = lax.axis_size(axis)
    pairs = [(source, (source + steps) % count) for source in range(count)]
    return lax.ppermute(value, axis, pairs)


def collect(value):
    count = lax.axis_size("sub")
    half = count // 2
    partner = lax.ppermute(value, "sub", [(i, i ^ 1) for i in range(count)])
    pair = jnp.stack([value, partner])
    parts = [pair]
    for k in range(1, half):
        moves = [(i, ((i // 2 + k) % half) * 2 + i % 2) for i in range(count)]
        parts.append(lax.ppermute(pair, "sub", moves))
    return jnp.stack(parts).reshape((count,) + value.shape)


def slot_of(index, me, count, chunk):
    owner = index // chunk
    slot = ((me // 2 - owner // 2) % (count // 2)) * 2 + ((owner % 2) ^ (me % 2))
    return slot * chunk + index % chunk


def apply_blocks(blocks, own_part, others):
    picked = jnp.concatenate([own_part, others], axis=1)
    result = jnp.sum(blocks[0] * picked[:, None, :], axis=2)
    return result.reshape(1, -1)


def next_hist(end_volt, hist, surge):
    outgoing_ends = jnp.stack([end_volt[:, 0], hist[:, 0]], axis=1)
    message = -2.0 * surge * end_volt[:, 1] - hist[:, 1]
    from_right, new_left = lax.optimization_barrier(
        (shifted(outgoing_ends, "area", -1), shifted(message, "area", 1)))
    new_right = -2.0 * surge * from_right[:, 0] - from_right[:, 1]
    return jnp.stack([new_left, new_right], axis=1)


def on_device(blocks, pattern, line_ends, sources, capacity, start_volt, start_hist, surge):
    width = blocks.shape[2]
    rows_here = blocks.shape[1]
    local_count = rows_here * width
    offset = lax.axis_index("sub") * local_count
    eye = jnp.arange(width)[:, None] == jnp.arange(width)[None, :]
    diag = jnp.sum(jnp.where(eye, blocks[0, :, :, :width], 0.0), axis=2).reshape(1, local_count)
    system_diag = diag + capacity
    count = lax.axis_size("sub")
    me = lax.axis_index("sub")
    remote_cols = slot_of(pattern[0][:, 1:].reshape(-1), me, count, rows_here)
    end_index = slot_of(line_ends[0], me, count, local_count)
    local_ends = line_ends - offset
    inside = (local_ends >= 0) & (local_ends < local_count)
    safe_ends = jnp.clip(local_ends, 0, local_count - 1)
    buses = jnp.arange(local_count)[None, :]
    at_bus = (safe_ends.reshape(-1, 1) == buses) & inside.reshape(-1, 1)
    volt = start_volt
    hist = start_hist
    for step in range(STEPS):
        field = volt
        rhs = None
        for sweep in range(SWEEPS):
            whole = collect(field.reshape(-1, 128))
            if rhs is None:
                if step > 0:
                    end_volt = whole.reshape(-1)[end_index][None]
                    hist = next_hist(end_volt, hist, surge)
                rhs = sources[step] + capacity * volt
                inject = jnp.where(at_bus, -hist.reshape(-1, 1), 0.0)
                rhs = rhs + jnp.sum(inject, axis=0, keepdims=True)
            own_part = field.reshape(rows_here, width)
            others = whole.reshape(-1, width)[remote_cols]
            others = others.reshape(rows_here, -1)
            result = apply_blocks(blocks, own_part, others)
            field = field + (rhs - result - capacity * field) / system_diag
        volt = field
    partial_volt = jnp.where(inside, volt[0][safe_ends[0]][None], 0.0)
    end_volt = jnp.sum(collect(partial_volt), axis=0)
    hist = next_hist(end_volt, hist, surge)
    return (volt, hist)


def solution(mesh):
    in_specs = (
        P("area", "sub", None, None),
        P("area", "sub", None),
        P("area", None, None),
        P(None, "area", "sub"),
        P("area", "sub"),
        P("area", "sub"),
        P("area", None, None),
        P("area", None),
    )
    out_specs = (P("area", "sub"), P("area", None, None))
    return jax.shard_map(
        on_device, mesh=mesh, in_specs=in_specs, out_specs=out_specs, check_vma=False
    )
```

```python
import jax
import jax.numpy as jnp
from jax import lax
from jax.sharding import PartitionSpec as P

STEPS = 4
SWEEPS = 8


def shifted(value, axis, steps):
    count = lax.axis_size(axis)
    pairs = [(source, (source + steps) % count) for source in range(count)]
    return lax.ppermute(value, axis, pairs)


def collect(value):
    count = lax.axis_size("sub")
    half = count // 2
    partner = lax.ppermute(value, "sub", [(i, i ^ 1) for i in range(count)])
    pair = jnp.stack([value, partner])
    parts = [pair]
    for k in range(1, half):
        moves = [(i, ((i // 2 + k) % half) * 2 + i % 2) for i in range(count)]
        parts.append(lax.ppermute(pair, "sub", moves))
    return jnp.stack(parts).reshape((count,) + value.shape)


def slot_of(index, me, count, chunk):
    owner = index // chunk
    slot = ((me // 2 - owner // 2) % (count // 2)) * 2 + ((owner % 2) ^ (me % 2))
    return slot * chunk + index % chunk


def apply_blocks(blocks, own_part, others):
    picked = jnp.concatenate([own_part, others], axis=1)
    result = jnp.sum(blocks[0] * picked[:, None, :], axis=2)
    return result.reshape(1, -1)


def next_hist(end_volt, hist, surge):
    outgoing_ends = jnp.stack([end_volt[:, 0], hist[:, 0]], axis=1)
    message = -2.0 * surge * end_volt[:, 1] - hist[:, 1]
    from_right, new_left = lax.optimization_barrier(
        (shifted(outgoing_ends, "area", -1), shifted(message, "area", 1)))
    new_right = -2.0 * surge * from_right[:, 0] - from_right[:, 1]
    return jnp.stack([new_left, new_right], axis=1)


def on_device(blocks, pattern, line_ends, sources, capacity, start_volt, start_hist, surge):
    width = blocks.shape[2]
    rows_here = blocks.shape[1]
    local_count = rows_here * width
    offset = lax.axis_index("sub") * local_count
    eye = jnp.arange(width)[:, None] == jnp.arange(width)[None, :]
    diag = jnp.sum(jnp.where(eye, blocks[0, :, :, :width], 0.0), axis=2).reshape(1, local_count)
    system_diag = diag + capacity
    count = lax.axis_size("sub")
    me = lax.axis_index("sub")
    remote_cols = slot_of(pattern[0][:, 1:].reshape(-1), me, count, rows_here)
    end_index = slot_of(line_ends[0], me, count, local_count)
    local_ends = line_ends - offset
    inside = (local_ends >= 0) & (local_ends < local_count)
    safe_ends = jnp.clip(local_ends, 0, local_count - 1)
    buses = jnp.arange(local_count)[None, :]
    at_bus = (safe_ends.reshape(-1, 1) == buses) & inside.reshape(-1, 1)
    volt = start_volt
    hist = start_hist
    for step in range(STEPS):
        field = volt
        rhs = None
        for sweep in range(SWEEPS):
            whole = collect(field.reshape(-1, 128))
            if rhs is None:
                if step > 0:
                    end_volt = whole.reshape(-1)[end_index][None]
                    hist = next_hist(end_volt, hist, surge)
                rhs = sources[step] + capacity * volt
                inject = jnp.where(at_bus, -hist.reshape(-1, 1), 0.0)
                rhs = rhs + jnp.sum(inject, axis=0, keepdims=True)
            own_part = field.reshape(rows_here, width)
            others = whole.reshape(-1, width)[remote_cols]
            others = others.reshape(rows_here, -1)
            result = apply_blocks(blocks, own_part, others)
            field = field + (rhs - result - capacity * field) / system_diag
        volt = field
    partial_volt = jnp.where(inside, volt[0][safe_ends[0]][None], 0.0)
    count = lax.axis_size("sub")
    copies = jnp.broadcast_to(partial_volt[None], (count,) + partial_volt.shape)
    end_volt = jnp.sum(lax.all_to_all(copies, "sub", 0, 0, tiled=True), axis=0)
    hist = next_hist(end_volt, hist, surge)
    return (volt, hist)


def solution(mesh):
    in_specs = (
        P("area", "sub", None, None),
        P("area", "sub", None),
        P("area", None, None),
        P(None, "area", "sub"),
        P("area", "sub"),
        P("area", "sub"),
        P("area", None, None),
        P("area", None),
    )
    out_specs = (P("area", "sub"), P("area", None, None))
    return jax.shard_map(
        on_device, mesh=mesh, in_specs=in_specs, out_specs=out_specs, check_vma=False
    )
```
